512 devices in a mesh: col: 4 (over x_lo, core), gx: 16 (over z), gy: 8 (over x_hi, y).
Axes of the slice: x: 4 (x_hi: 2, x_lo: 2; x = x_hi * 2 + x_lo), y: 4, z: 16, core: 2. Of those that a mesh axis runs over, the one named last changes fastest.
Arguments:
- volume: float32 [32, 8, 64, 1024], P('col', None, 'gx', 'gy'), may hold values from -6 to 6
- filters: float32 [32, 32, 3, 3, 3], P('col'), may hold values from -0.21875 to 0.21875
- upstream: float32 [32, 8, 64, 1024], P('col', None, 'gx', 'gy'), may hold values from -6 to 6
Outputs:
- response: float32 [32, 8, 64, 1024], P('col', None, 'gx', 'gy')
- input_grad: float32 [32, 8, 64, 1024], P('col', None, 'gx', 'gy')
- filter_grad: float32 [32, 32, 3, 3, 3], P('col')
The draws below stay inside these ranges and needn't reach their ends.
All inputs are finite; a program needn't handle non-finite values.
Results may differ from the reference program's by a relative error of at most 0.0003.
Values sent between devices are 32-bit elements; how exact they have to be, the bound alone decides.
No kernel may reach another device: no remote copies, remote signals or barrier semaphores. Data moves between devices by JAX's collectives and lax.ppermute only.
A program may use at most 64 MiB of HBM per device.

```python
import jax
import jax.numpy as jnp
from jax import lax

C_IN = 32
C_OUT = 32
PLANES = 8
NX = 64
NY = 1024


def steps_of(rng, shape, pieces, smallest, top_value):
    loudness = 1.0
    for position, shards_of in pieces:
        heights = jax.random.uniform(jax.random.fold_in(jax.random.fold_in(rng, 6), position), (shards_of,), jnp.float32, smallest / len(pieces), top_value / len(pieces))
        loudness = loudness * jnp.repeat(jnp.exp(heights), shape[position] // shards_of).reshape((-1,) + (1,) * (len(shape) - 1 - position))
    return loudness


def scatter_about(key, shape, scale, reach, cuts=(), kind=jnp.bfloat16):
    values = scale * jax.random.normal(key, shape, jnp.float32)
    if cuts:
        values = values * steps_of(key, shape, cuts, -0.22, 0.18)
    return jnp.clip(values, -reach, reach).astype(kind)


def setup_inputs(seed: int = 0) -> dict:
    streams_of = jax.random.split(jax.random.key(seed), 4)
    return {
        "volume": scatter_about(streams_of[0], (C_IN, PLANES, NX, NY), 1.0, 6.0, ((0, 4), (2, 16), (3, 8)), jnp.float32),
        "filters": scatter_about(streams_of[1], (C_OUT, C_IN, 3, 3, 3), (C_IN * 27) ** -0.5, 0.21875, ((0, 4),), jnp.float32),
        "upstream": scatter_about(streams_of[2], (C_OUT, PLANES, NX, NY), 1.0, 6.0, ((0, 4), (2, 16), (3, 8)), jnp.float32),
    }


def convolve(volume, filters):
    result = lax.conv_general_dilated(volume[None], filters, (1, 1, 1), ((1, 1), (1, 1), (1, 1)), dimension_numbers=('NCDHW', 'OIDHW', 'NCDHW'), precision=lax.Precision.HIGHEST)
    return result[0]

def reference(volume, filters, upstream):
    response, backward = jax.vjp(convolve, volume, filters)
    input_grad, weight_total = backward(upstream)
    scale = (PLANES * NX * NY) ** (-0.5)
    return (response, input_grad, weight_total * scale)
```

```python
import jax
import jax.numpy as jnp
from jax import lax
from jax.sharding import PartitionSpec as P


def with_halo(block, sides, width):
    for axis, dim in sides:
        count = lax.axis_size(axis)
        forward = [(i, i + 1) for i in range(count - 1)]
        backward = [(target, source) for source, target in forward]
        low = lax.ppermute(
            lax.slice_in_dim(block, block.shape[dim] - width, None, axis=dim), axis, forward
        )
        high = lax.ppermute(lax.slice_in_dim(block, 0, width, axis=dim), axis, backward)
        block = jnp.concatenate([low, block, high], axis=dim)
    return block


def pad_depth(field):
    return jnp.pad(field, ((0, 0), (1, 1), (0, 0), (0, 0)))


def forward_conv(padded, weights, planes, rows_x, rows_y):
    output = jnp.zeros((weights.shape[0], planes, rows_x, rows_y), jnp.float32)
    for depth in range(3):
        for across in range(3):
            for along in range(3):
                window = padded[
                    :, depth : depth + planes, across : across + rows_x, along : along + rows_y
                ]
                output = output + jnp.einsum(
                    "oc,czxy->ozxy",
                    weights[:, :, depth, across, along],
                    window,
                    precision=lax.Precision.HIGHEST,
                )
    return output


def backward_conv(padded_up, weights, planes, rows_x, rows_y):
    output = jnp.zeros((weights.shape[1], planes, rows_x, rows_y), jnp.float32)
    for depth in range(3):
        for across in range(3):
            for along in range(3):
                window = padded_up[
                    :,
                    2 - depth : 2 - depth + planes,
                    2 - across : 2 - across + rows_x,
                    2 - along : 2 - along + rows_y,
                ]
                output = output + jnp.einsum(
                    "oc,ozxy->czxy",
                    weights[:, :, depth, across, along],
                    window,
                    precision=lax.Precision.HIGHEST,
                )
    return output


def weight_terms(cotangent, padded, planes, rows_x, rows_y):
    pieces = []
    for depth in range(3):
        for across in range(3):
            for along in range(3):
                window = padded[
                    :, depth : depth + planes, across : across + rows_x, along : along + rows_y
                ]
                pieces.append(
                    jnp.einsum("ozxy,czxy->oc", cotangent, window, precision=lax.Precision.HIGHEST)
                )
    stacked = jnp.stack(pieces, axis=-1)
    return stacked.reshape(stacked.shape[0], stacked.shape[1], 3, 3, 3)


def shards(volume, filters, upstream):
    planes, rows_x, rows_y = (volume.shape[1], volume.shape[2], volume.shape[3])
    own_inputs = volume.shape[0]
    scale = (planes * rows_x * lax.axis_size("gx") * rows_y * lax.axis_size("gy")) ** (-0.5)
    gathered = lax.all_gather(volume, "col", axis=0, tiled=True)
    padded = pad_depth(with_halo(gathered, (("gx", 2), ("gy", 3)), 1))
    response = forward_conv(padded, filters, planes, rows_x, rows_y)
    all_rows = lax.all_gather(filters, "col", axis=0, tiled=True)
    all_upstream = lax.all_gather(upstream, "col", axis=0, tiled=True)
    padded_up = pad_depth(with_halo(all_upstream, (("gx", 2), ("gy", 3)), 1))
    first = lax.axis_index("col") * own_inputs
    own_filters = lax.dynamic_slice_in_dim(all_rows, first, own_inputs, 1)
    input_grad = backward_conv(padded_up, own_filters, planes, rows_x, rows_y)
    local_grad = weight_terms(upstream, padded, planes, rows_x, rows_y)
    ncol = lax.axis_size("col")
    flat = local_grad.reshape(-1, 128)
    slots = jnp.zeros((ncol,) + flat.shape, jnp.float32)
    slots = lax.dynamic_update_index_in_dim(slots, flat, lax.axis_index("col"), 0)
    summed = lax.psum(slots, ("col", "gx", "gy"))
    total_grad = summed[lax.axis_index("col")].reshape(local_grad.shape)
    return (response, input_grad, total_grad * scale)


def solution(mesh):
    placed = (
        P("col", None, "gx", "gy"),
        P("col", None, None, None, None),
        P("col", None, "gx", "gy"),
    )
    return jax.shard_map(
        shards,
        mesh=mesh,
        in_specs=placed,
        out_specs=(
            P("col", None, "gx", "gy"),
            P("col", None, "gx", "gy"),
            P("col", None, None, None, None),
        ),
        check_vma=False,
    )
```

```python
import jax
import jax.numpy as jnp
from jax import lax
from jax.sharding import PartitionSpec as P


def with_halo(block, sides, width):
    for axis, dim in sides:
        count = lax.axis_size(axis)
        forward = [(i, i + 1) for i in range(count - 1)]
        backward = [(target, source) for source, target in forward]
        low = lax.ppermute(
            lax.slice_in_dim(block, block.shape[dim] - width, None, axis=dim), axis, forward
        )
        high = lax.ppermute(lax.slice_in_dim(block, 0, width, axis=dim), axis, backward)
        block = jnp.concatenate([low, block, high], axis=dim)
    return block


def butterfly_sum(value, axes):
    for axis in axes:
        count = lax.axis_size(axis)
        step = 1
        while step < count:
            pairs = [(i, i ^ step) for i in range(count)]
            value = value + lax.ppermute(value, axis, pairs)
            step *= 2
    return value


def pad_depth(field):
    return jnp.pad(field, ((0, 0), (1, 1), (0, 0), (0, 0)))


def forward_conv(padded, weights, planes, rows_x, rows_y):
    output = jnp.zeros((weights.shape[0], planes, rows_x, rows_y), jnp.float32)
    for depth in range(3):
        for across in range(3):
            for along in range(3):
                window = padded[
                    :, depth : depth + planes, across : across + rows_x, along : along + rows_y
                ]
                output = output + jnp.einsum(
                    "oc,czxy->ozxy",
                    weights[:, :, depth, across, along],
                    window,
                    precision=lax.Precision.HIGHEST,
                )
    return output


def backward_conv(padded_up, weights, planes, rows_x, rows_y):
    output = jnp.zeros((weights.shape[1], planes, rows_x, rows_y), jnp.float32)
    for depth in range(3):
        for across in range(3):
            for along in range(3):
                window = padded_up[
                    :,
                    2 - depth : 2 - depth + planes,
                    2 - across : 2 - across + rows_x,
                    2 - along : 2 - along + rows_y,
                ]
                output = output + jnp.einsum(
                    "oc,ozxy->czxy",
                    weights[:, :, depth, across, along],
                    window,
                    precision=lax.Precision.HIGHEST,
                )
    return output


def weight_terms(cotangent, padded, planes, rows_x, rows_y):
    pieces = []
    for depth in range(3):
        for across in range(3):
            for along in range(3):
                window = padded[
                    :, depth : depth + planes, across : across + rows_x, along : along + rows_y
                ]
                pieces.append(
                    jnp.einsum("ozxy,czxy->oc", cotangent, window, precision=lax.Precision.HIGHEST)
                )
    stacked = jnp.stack(pieces, axis=-1)
    return stacked.reshape(stacked.shape[0], stacked.shape[1], 3, 3, 3)


def shards(volume, filters, upstream):
    planes, rows_x, rows_y = (volume.shape[1], volume.shape[2], volume.shape[3])
    own_inputs = volume.shape[0]
    scale = (planes * rows_x * lax.axis_size("gx") * rows_y * lax.axis_size("gy")) ** (-0.5)
    gathered = lax.all_gather(volume, "col", axis=0, tiled=True)
    padded = pad_depth(with_halo(gathered, (("gx", 2), ("gy", 3)), 1))
    response = forward_conv(padded, filters, planes, rows_x, rows_y)
    all_rows = lax.all_gather(filters, "col", axis=0, tiled=True)
    all_upstream = lax.all_gather(upstream, "col", axis=0, tiled=True)
    padded_up = pad_depth(with_halo(all_upstream, (("gx", 2), ("gy", 3)), 1))
    first = lax.axis_index("col") * own_inputs
    own_filters = lax.dynamic_slice_in_dim(all_rows, first, own_inputs, 1)
    input_grad = backward_conv(padded_up, own_filters, planes, rows_x, rows_y)
    local_grad = weight_terms(upstream, padded, planes, rows_x, rows_y)
    flat = local_grad.reshape(-1, 128)
    sizes = [lax.axis_size(a) for a in ("gx", "gy")]
    if all(n & (n - 1) == 0 for n in sizes):
        flat = butterfly_sum(flat, ("gx", "gy"))
    else:
        flat = lax.psum(flat, ("gx", "gy"))
    total_grad = flat.reshape(local_grad.shape)
    return (response, input_grad, total_grad * scale)


def solution(mesh):
    placed = (
        P("col", None, "gx", "gy"),
        P("col", None, None, None, None),
        P("col", None, "gx", "gy"),
    )
    return jax.shard_map(
        shards,
        mesh=mesh,
        in_specs=placed,
        out_specs=(
            P("col", None, "gx", "gy"),
            P("col", None, "gx", "gy"),
            P("col", None, None, None, None),
        ),
        check_vma=False,
    )
```

```python
import jax
import jax.numpy as jnp
from jax import lax
from jax.sharding import PartitionSpec as P


def with_halo(block, sides, width):
    for axis, dim in sides:
        count = lax.axis_size(axis)
        forward = [(i, i + 1) for i in range(count - 1)]
        backward = [(target, source) for source, target in forward]
        low = lax.ppermute(
            lax.slice_in_dim(block, block.shape[dim] - width, None, axis=dim), axis, forward
        )
        high = lax.ppermute(lax.slice_in_dim(block, 0, width, axis=dim), axis, backward)
        block = jnp.concatenate([low, block, high], axis=dim)
    return block


def butterfly_sum(value, axes):
    for axis in axes:
        count = lax.axis_size(axis)
        step = 1
        while step < count:
            pairs = [(i, i ^ step) for i in range(count)]
            value = value + lax.ppermute(value, axis, pairs)
            step *= 2
    return value


def pad_depth(field):
    return jnp.pad(field, ((0, 0), (1, 1), (0, 0), (0, 0)))


def conv_valid(field, weights):
    return lax.conv_general_dilated(
        field[None],
        weights,
        (1, 1, 1),
        "VALID",
        dimension_numbers=("NCDHW", "OIDHW", "NCDHW"),
        precision=lax.Precision.HIGHEST,
    )[0]


def shards(volume, filters, upstream):
    planes, rows_x, rows_y = (volume.shape[1], volume.shape[2], volume.shape[3])
    own_inputs = volume.shape[0]
    scale = (planes * rows_x * lax.axis_size("gx") * rows_y * lax.axis_size("gy")) ** (-0.5)
    gathered = lax.all_gather(volume, "col", axis=0, tiled=True)
    padded = pad_depth(with_halo(gathered, (("gx", 2), ("gy", 3)), 1))
    response, filter_vjp = jax.vjp(lambda w: conv_valid(padded, w), filters)
    all_rows = lax.all_gather(filters, "col", axis=0, tiled=True)
    all_upstream = lax.all_gather(upstream, "col", axis=0, tiled=True)
    padded_up = pad_depth(with_halo(all_upstream, (("gx", 2), ("gy", 3)), 1))
    first = lax.axis_index("col") * own_inputs
    own_filters = lax.dynamic_slice_in_dim(all_rows, first, own_inputs, 1)
    turned = jnp.flip(jnp.swapaxes(own_filters, 0, 1), axis=(2, 3, 4))
    input_grad = conv_valid(padded_up, turned)
    (local_grad,) = filter_vjp(upstream)
    flat = local_grad.reshape(-1, 128)
    sizes = [lax.axis_size(a) for a in ("gx", "gy")]
    if all(n & (n - 1) == 0 for n in sizes):
        flat = butterfly_sum(flat, ("gx", "gy"))
    else:
        flat = lax.psum(flat, ("gx", "gy"))
    total_grad = flat.reshape(local_grad.shape)
    return (response, input_grad, total_grad * scale)


def solution(mesh):
    placed = (
        P("col", None, "gx", "gy"),
        P("col", None, None, None, None),
        P("col", None, "gx", "gy"),
    )
    return jax.shard_map(
        shards,
        mesh=mesh,
        in_specs=placed,
        out_specs=(
            P("col", None, "gx", "gy"),
            P("col", None, "gx", "gy"),
            P("col", None, None, None, None),
        ),
        check_vma=False,
    )
```

```python
import jax
import jax.numpy as jnp
from jax import lax
from jax.sharding import PartitionSpec as P


def with_halo(block, sides, width):
    for axis, dim in sides:
        count = lax.axis_size(axis)
        forward = [(i, i + 1) for i in range(count - 1)]
        backward = [(target, source) for source, target in forward]
        low = lax.ppermute(
            lax.slice_in_dim(block, block.shape[dim] - width, None, axis=dim), axis, forward
        )
        high = lax.ppermute(lax.slice_in_dim(block, 0, width, axis=dim), axis, backward)
        block = jnp.concatenate([low, block, high], axis=dim)
    return block


def butterfly_sum(value, axes):
    for axis in axes:
        count = lax.axis_size(axis)
        step = 1
        while step < count:
            pairs = [(i, i ^ step) for i in range(count)]
            value = value + lax.ppermute(value, axis, pairs)
            step *= 2
    return value


def pad_depth(field):
    return jnp.pad(field, ((0, 0), (1, 1), (0, 0), (0, 0)))


def patches(field, planes, rows_x, rows_y, flip):
    windows = []
    for depth in range(3):
        for across in range(3):
            for along in range(3):
                a, b, e = (2 - depth, 2 - across, 2 - along) if flip else (depth, across, along)
                windows.append(field[:, a : a + planes, b : b + rows_x, e : e + rows_y])
    return jnp.stack(windows, axis=0)


def shards(volume, filters, upstream):
    planes, rows_x, rows_y = (volume.shape[1], volume.shape[2], volume.shape[3])
    own_inputs = volume.shape[0]
    scale = (planes * rows_x * lax.axis_size("gx") * rows_y * lax.axis_size("gy")) ** (-0.5)
    gathered = lax.all_gather(volume, "col", axis=0, tiled=True)
    padded = pad_depth(with_halo(gathered, (("gx", 2), ("gy", 3)), 1))
    taps = patches(padded, planes, rows_x, rows_y, False)
    by_tap = jnp.swapaxes(filters.reshape(filters.shape[0], filters.shape[1], 27), 1, 2)
    response = jnp.einsum("okc,kcpqy->opqy", by_tap, taps, precision=lax.Precision.HIGHEST)
    all_rows = lax.all_gather(filters, "col", axis=0, tiled=True)
    all_upstream = lax.all_gather(upstream, "col", axis=0, tiled=True)
    padded_up = pad_depth(with_halo(all_upstream, (("gx", 2), ("gy", 3)), 1))
    first = lax.axis_index("col") * own_inputs
    own_filters = lax.dynamic_slice_in_dim(all_rows, first, own_inputs, 1)
    own_by_tap = jnp.swapaxes(own_filters.reshape(own_filters.shape[0], own_inputs, 27), 1, 2)
    taps_up = patches(padded_up, planes, rows_x, rows_y, True)
    input_grad = jnp.einsum("okc,kopqy->cpqy", own_by_tap, taps_up, precision=lax.Precision.HIGHEST)
    local_grad = jnp.einsum("opqy,kcpqy->ock", upstream, taps, precision=lax.Precision.HIGHEST)
    local_grad = local_grad.reshape(local_grad.shape[0], local_grad.shape[1], 3, 3, 3)
    flat = local_grad.reshape(-1, 128)
    sizes = [lax.axis_size(a) for a in ("gx", "gy")]
    if all(n & (n - 1) == 0 for n in sizes):
        flat = butterfly_sum(flat, ("gx", "gy"))
    else:
        flat = lax.psum(flat, ("gx", "gy"))
    total_grad = flat.reshape(local_grad.shape)
    return (response, input_grad, total_grad * scale)


def solution(mesh):
    placed = (
        P("col", None, "gx", "gy"),
        P("col", None, None, None, None),
        P("col", None, "gx", "gy"),
    )
    return jax.shard_map(
        shards,
        mesh=mesh,
        in_specs=placed,
        out_specs=(
            P("col", None, "gx", "gy"),
            P("col", None, "gx", "gy"),
            P("col", None, None, None, None),
        ),
        check_vma=False,
    )
```

```python
import jax
import jax.numpy as jnp
from jax import lax
from jax.sharding import PartitionSpec as P


def with_halo(block, sides, width):
    for axis, dim in sides:
        count = lax.axis_size(axis)
        forward = [(i, i + 1) for i in range(count - 1)]
        backward = [(target, source) for source, target in forward]
        low = lax.ppermute(
            lax.slice_in_dim(block, block.shape[dim] - width, None, axis=dim), axis, forward
        )
        high = lax.ppermute(lax.slice_in_dim(block, 0, width, axis=dim), axis, backward)
        block = jnp.concatenate([low, block, high], axis=dim)
    return block


def butterfly_sum(value, axes):
    for axis in axes:
        count = lax.axis_size(axis)
        step = 1
        while step < count:
            pairs = [(i, i ^ step) for i in range(count)]
            value = value + lax.ppermute(value, axis, pairs)
            step *= 2
    return value


def pad_depth(field):
    return jnp.pad(field, ((0, 0), (1, 1), (0, 0), (0, 0)))


def patches(field, planes, rows_x, rows_y, flip):
    windows = []
    for depth in range(3):
        for across in range(3):
            for along in range(3):
                a, b, e = (2 - depth, 2 - across, 2 - along) if flip else (depth, across, along)
                windows.append(field[:, a : a + planes, b : b + rows_x, e : e + rows_y])
    return jnp.stack(windows, axis=0)


def shards(volume, filters, upstream):
    channels, planes, rows_x, rows_y = volume.shape
    own_inputs = channels
    ncol = lax.axis_size("col")
    scale = (planes * rows_x * lax.axis_size("gx") * rows_y * lax.axis_size("gy")) ** (-0.5)
    cells = volume.size
    joined = jnp.concatenate([volume.reshape(-1), upstream.reshape(-1), filters.reshape(-1)])
    every = lax.all_gather(joined, "col", axis=0, tiled=False)
    fields = every[:, : 2 * cells].reshape(ncol, 2, channels, planes, rows_x, rows_y)
    fields = jnp.swapaxes(fields, 0, 1).reshape(2, ncol * channels, planes, rows_x, rows_y)
    all_rows = every[:, 2 * cells :].reshape((ncol * filters.shape[0],) + filters.shape[1:])
    both = with_halo(fields, (("gx", 3), ("gy", 4)), 1)
    both = jnp.pad(both, ((0, 0), (0, 0), (1, 1), (0, 0), (0, 0)))
    padded, padded_up = both[0], both[1]
    taps = patches(padded, planes, rows_x, rows_y, False)
    local_grad = jnp.einsum("opqy,kcpqy->ock", upstream, taps, precision=lax.Precision.HIGH)
    local_grad = local_grad.reshape(local_grad.shape[0], local_grad.shape[1], 3, 3, 3)
    flat = local_grad.reshape(-1, 128)
    sizes = [lax.axis_size(a) for a in ("gx", "gy")]
    if all(n & (n - 1) == 0 for n in sizes):
        flat = butterfly_sum(flat, ("gx", "gy"))
    else:
        flat = lax.psum(flat, ("gx", "gy"))
    total_grad = flat.reshape(local_grad.shape)
    by_tap = jnp.swapaxes(filters.reshape(filters.shape[0], filters.shape[1], 27), 1, 2)
    response = jnp.einsum("okc,kcpqy->opqy", by_tap, taps, precision=lax.Precision.HIGH)
    first = lax.axis_index("col") * own_inputs
    own_filters = lax.dynamic_slice_in_dim(all_rows, first, own_inputs, 1)
    own_by_tap = jnp.swapaxes(own_filters.reshape(own_filters.shape[0], own_inputs, 27), 1, 2)
    taps_up = patches(padded_up, planes, rows_x, rows_y, True)
    input_grad = jnp.einsum("okc,kopqy->cpqy", own_by_tap, taps_up, precision=lax.Precision.HIGH)
    return (response, input_grad, total_grad * scale)


def solution(mesh):
    placed = (
        P("col", None, "gx", "gy"),
        P("col", None, None, None, None),
        P("col", None, "gx", "gy"),
    )
    return jax.shard_map(
        shards,
        mesh=mesh,
        in_specs=placed,
        out_specs=(
            P("col", None, "gx", "gy"),
            P("col", None, "gx", "gy"),
            P("col", None, None, None, None),
        ),
        check_vma=False,
    )
```

```python
import jax
import jax.numpy as jnp
from jax import lax
from jax.sharding import PartitionSpec as P


def with_halo(block, sides, width):
    for axis, dim in sides:
        count = lax.axis_size(axis)
        forward = [(i, i + 1) for i in range(count - 1)]
        backward = [(target, source) for source, target in forward]
        low = lax.ppermute(
            lax.slice_in_dim(block, block.shape[dim] - width, None, axis=dim), axis, forward
        )
        high = lax.ppermute(lax.slice_in_dim(block, 0, width, axis=dim), axis, backward)
        block = jnp.concatenate([low, block, high], axis=dim)
    return block


def butterfly_sum(value, axes):
    for axis in axes:
        count = lax.axis_size(axis)
        index = lax.axis_index(axis)
        stride = 1
        while stride < count:
            radix = 4 if (count // stride) % 4 == 0 else 2
            member = (index // stride) % radix
            received = [value]
            for shift in range(1, radix):
                pairs = []
                for i in range(count):
                    m = (i // stride) % radix
                    j = i + (((m + shift) % radix) - m) * stride
                    pairs.append((i, j))
                received.append(lax.ppermute(value, axis, pairs))
            stacked = jnp.stack(received)
            ordered = jnp.take(stacked, (member - jnp.arange(radix)) % radix, axis=0)
            parts = [ordered[m] for m in range(radix)]
            while len(parts) > 1:
                parts = [parts[k] + parts[k + 1] for k in range(0, len(parts), 2)]
            value = parts[0]
            stride *= radix
    return value


def pad_depth(field):
    return jnp.pad(field, ((0, 0), (1, 1), (0, 0), (0, 0)))


def patches(field, planes, rows_x, rows_y, flip):
    windows = []
    for depth in range(3):
        for across in range(3):
            for along in range(3):
                a, b, e = (2 - depth, 2 - across, 2 - along) if flip else (depth, across, along)
                windows.append(field[:, a : a + planes, b : b + rows_x, e : e + rows_y])
    return jnp.stack(windows, axis=0)


def shards(volume, filters, upstream):
    channels, planes, rows_x, rows_y = volume.shape
    own_inputs = channels
    ncol = lax.axis_size("col")
    scale = (planes * rows_x * lax.axis_size("gx") * rows_y * lax.axis_size("gy")) ** (-0.5)
    fields = jnp.stack(
        [lax.all_gather(volume, "col", axis=0, tiled=True),
         lax.all_gather(upstream, "col", axis=0, tiled=True)]
    )
    all_rows = lax.all_gather(filters, "col", axis=0, tiled=True)
    both = with_halo(fields, (("gx", 3), ("gy", 4)), 1)
    both = jnp.pad(both, ((0, 0), (0, 0), (1, 1), (0, 0), (0, 0)))
    padded, padded_up = both[0], both[1]
    taps = patches(padded, planes, rows_x, rows_y, False)
    local_grad = jnp.einsum("opqy,kcpqy->ock", upstream, taps, precision=lax.Precision.HIGH)
    local_grad = local_grad.reshape(local_grad.shape[0], local_grad.shape[1], 3, 3, 3)
    flat = local_grad.reshape(-1, 128)
    sizes = [lax.axis_size(a) for a in ("gx", "gy")]
    if all(n & (n - 1) == 0 for n in sizes):
        flat = butterfly_sum(flat, ("gx", "gy"))
    else:
        flat = lax.psum(flat, ("gx", "gy"))
    total_grad = flat.reshape(local_grad.shape)
    by_tap = jnp.swapaxes(filters.reshape(filters.shape[0], filters.shape[1], 27), 1, 2)
    response = jnp.einsum("okc,kcpqy->opqy", by_tap, taps, precision=lax.Precision.HIGH)
    first = lax.axis_index("col") * own_inputs
    own_filters = lax.dynamic_slice_in_dim(all_rows, first, own_inputs, 1)
    own_by_tap = jnp.swapaxes(own_filters.reshape(own_filters.shape[0], own_inputs, 27), 1, 2)
    taps_up = patches(padded_up, planes, rows_x, rows_y, True)
    input_grad = jnp.einsum("okc,kopqy->cpqy", own_by_tap, taps_up, precision=lax.Precision.HIGH)
    return (response, input_grad, total_grad * scale)


def solution(mesh):
    placed = (
        P("col", None, "gx", "gy"),
        P("col", None, None, None, None),
        P("col", None, "gx", "gy"),
    )
    return jax.shard_map(
        shards,
        mesh=mesh,
        in_specs=placed,
        out_specs=(
            P("col", None, "gx", "gy"),
            P("col", None, "gx", "gy"),
            P("col", None, None, None, None),
        ),
        check_vma=False,
    )
```

```python
import jax
import jax.numpy as jnp
from jax import lax
from jax.sharding import PartitionSpec as P


def with_halo(block, sides, width):
    for axis, dim in sides:
        count = lax.axis_size(axis)
        forward = [(i, i + 1) for i in range(count - 1)]
        backward = [(target, source) for source, target in forward]
        low = lax.ppermute(
            lax.slice_in_dim(block, block.shape[dim] - width, None, axis=dim), axis, forward
        )
        high = lax.ppermute(lax.slice_in_dim(block, 0, width, axis=dim), axis, backward)
        block = jnp.concatenate([low, block, high], axis=dim)
    return block


def butterfly_sum(value, axes):
    for axis in axes:
        count = lax.axis_size(axis)
        index = lax.axis_index(axis)
        stride = 1
        while stride < count:
            radix = 4 if (count // stride) % 4 == 0 else 2
            member = (index // stride) % radix
            received = [value]
            for shift in range(1, radix):
                pairs = []
                for i in range(count):
                    m = (i // stride) % radix
                    j = i + (((m + shift) % radix) - m) * stride
                    pairs.append((i, j))
                received.append(lax.ppermute(value, axis, pairs))
            stacked = jnp.stack(received)
            ordered = jnp.take(stacked, (member - jnp.arange(radix)) % radix, axis=0)
            parts = [ordered[m] for m in range(radix)]
            while len(parts) > 1:
                parts = [parts[k] + parts[k + 1] for k in range(0, len(parts), 2)]
            value = parts[0]
            stride *= radix
    return value


def pad_depth(field):
    return jnp.pad(field, ((0, 0), (1, 1), (0, 0), (0, 0)))


def patches(field, planes, rows_x, rows_y, flip):
    windows = []
    for depth in range(3):
        for across in range(3):
            for along in range(3):
                a, b, e = (2 - depth, 2 - across, 2 - along) if flip else (depth, across, along)
                windows.append(field[:, a : a + planes, b : b + rows_x, e : e + rows_y])
    return jnp.stack(windows, axis=0)


def shards(volume, filters, upstream):
    channels, planes, rows_x, rows_y = volume.shape
    own_inputs = channels
    ncol = lax.axis_size("col")
    scale = (planes * rows_x * lax.axis_size("gx") * rows_y * lax.axis_size("gy")) ** (-0.5)
    taps_per_row = filters[0].size
    rows_per_plane = rows_x * rows_y
    filter_planes = -(-taps_per_row // rows_per_plane)
    packed = jnp.pad(filters.reshape(channels, taps_per_row),
                     ((0, 0), (0, filter_planes * rows_per_plane - taps_per_row)))
    packed = packed.reshape(channels, filter_planes, rows_x, rows_y)
    joined = jnp.concatenate([volume, packed], axis=1)
    every = lax.all_gather(joined, "col", axis=0, tiled=True)
    fields = jnp.stack([every[:, :planes], lax.all_gather(upstream, "col", axis=0, tiled=True)])
    all_rows = every[:, planes:].reshape(every.shape[0], -1)[:, :taps_per_row]
    all_rows = all_rows.reshape((every.shape[0],) + filters.shape[1:])
    both = with_halo(fields, (("gx", 3), ("gy", 4)), 1)
    both = jnp.pad(both, ((0, 0), (0, 0), (1, 1), (0, 0), (0, 0)))
    padded, padded_up = both[0], both[1]
    taps = patches(padded, planes, rows_x, rows_y, False)
    local_grad = jnp.einsum("opqy,kcpqy->ock", upstream, taps, precision=lax.Precision.HIGH)
    local_grad = local_grad.reshape(local_grad.shape[0], local_grad.shape[1], 3, 3, 3)
    flat = local_grad.reshape(-1, 128)
    sizes = [lax.axis_size(a) for a in ("gx", "gy")]
    if all(n & (n - 1) == 0 for n in sizes):
        flat = butterfly_sum(flat, ("gx", "gy"))
    else:
        flat = lax.psum(flat, ("gx", "gy"))
    total_grad = flat.reshape(local_grad.shape)
    by_tap = jnp.swapaxes(filters.reshape(filters.shape[0], filters.shape[1], 27), 1, 2)
    response = jnp.einsum("okc,kcpqy->opqy", by_tap, taps, precision=lax.Precision.HIGH)
    first = lax.axis_index("col") * own_inputs
    own_filters = lax.dynamic_slice_in_dim(all_rows, first, own_inputs, 1)
    own_by_tap = jnp.swapaxes(own_filters.reshape(own_filters.shape[0], own_inputs, 27), 1, 2)
    taps_up = patches(padded_up, planes, rows_x, rows_y, True)
    input_grad = jnp.einsum("okc,kopqy->cpqy", own_by_tap, taps_up, precision=lax.Precision.HIGH)
    return (response, input_grad, total_grad * scale)


def solution(mesh):
    placed = (
        P("col", None, "gx", "gy"),
        P("col", None, None, None, None),
        P("col", None, "gx", "gy"),
    )
    return jax.shard_map(
        shards,
        mesh=mesh,
        in_specs=placed,
        out_specs=(
            P("col", None, "gx", "gy"),
            P("col", None, "gx", "gy"),
            P("col", None, None, None, None),
        ),
        check_vma=False,
    )
```

```python
import jax
import jax.numpy as jnp
from jax import lax
from jax.sharding import PartitionSpec as P


def with_halo(block, sides, width):
    for axis, dim in sides:
        count = lax.axis_size(axis)
        forward = [(i, i + 1) for i in range(count - 1)]
        backward = [(target, source) for source, target in forward]
        low = lax.ppermute(
            lax.slice_in_dim(block, block.shape[dim] - width, None, axis=dim), axis, forward
        )
        high = lax.ppermute(lax.slice_in_dim(block, 0, width, axis=dim), axis, backward)
        block = jnp.concatenate([low, block, high], axis=dim)
    return block


def neighbour(piece, dx, dy):
    nx, ny = lax.axis_size("gx"), lax.axis_size("gy")
    pairs = [
        (i * ny + j, (i + dx) * ny + (j + dy))
        for i in range(nx)
        for j in range(ny)
        if 0 <= i + dx < nx and 0 <= j + dy < ny
    ]
    return lax.ppermute(piece, ("gx", "gy"), pairs)


def with_halo_2d(block, dx_dim, dy_dim):
    def cut(x_at, y_at):
        piece = block
        if x_at is not None:
            piece = lax.slice_in_dim(piece, x_at, x_at + 1, axis=dx_dim)
        if y_at is not None:
            piece = lax.slice_in_dim(piece, y_at, y_at + 1, axis=dy_dim)
        return piece

    last_x, last_y = block.shape[dx_dim] - 1, block.shape[dy_dim] - 1
    low_x = neighbour(cut(last_x, None), 1, 0)
    high_x = neighbour(cut(0, None), -1, 0)
    low_y = neighbour(cut(None, last_y), 0, 1)
    high_y = neighbour(cut(None, 0), 0, -1)
    low_low = neighbour(cut(last_x, last_y), 1, 1)
    low_high = neighbour(cut(last_x, 0), 1, -1)
    high_low = neighbour(cut(0, last_y), -1, 1)
    high_high = neighbour(cut(0, 0), -1, -1)
    top = jnp.concatenate([low_low, low_x, low_high], axis=dy_dim)
    middle = jnp.concatenate([low_y, block, high_y], axis=dy_dim)
    bottom = jnp.concatenate([high_low, high_x, high_high], axis=dy_dim)
    return jnp.concatenate([top, middle, bottom], axis=dx_dim)


def butterfly_sum(value, axes):
    for axis in axes:
        count = lax.axis_size(axis)
        index = lax.axis_index(axis)
        stride = 1
        while stride < count:
            radix = 4 if (count // stride) % 4 == 0 else 2
            member = (index // stride) % radix
            received = [value]
            for shift in range(1, radix):
                pairs = []
                for i in range(count):
                    m = (i // stride) % radix
                    j = i + (((m + shift) % radix) - m) * stride
                    pairs.append((i, j))
                received.append(lax.ppermute(value, axis, pairs))
            stacked = jnp.stack(received)
            ordered = jnp.take(stacked, (member - jnp.arange(radix)) % radix, axis=0)
            parts = [ordered[m] for m in range(radix)]
            while len(parts) > 1:
                parts = [parts[k] + parts[k + 1] for k in range(0, len(parts), 2)]
            value = parts[0]
            stride *= radix
    return value


def pad_depth(field):
    return jnp.pad(field, ((0, 0), (1, 1), (0, 0), (0, 0)))


def patches(field, planes, rows_x, rows_y, flip):
    windows = []
    for depth in range(3):
        for across in range(3):
            for along in range(3):
                a, b, e = (2 - depth, 2 - across, 2 - along) if flip else (depth, across, along)
                windows.append(field[:, a : a + planes, b : b + rows_x, e : e + rows_y])
    return jnp.stack(windows, axis=0)


def shards(volume, filters, upstream):
    channels, planes, rows_x, rows_y = volume.shape
    own_inputs = channels
    ncol = lax.axis_size("col")
    scale = (planes * rows_x * lax.axis_size("gx") * rows_y * lax.axis_size("gy")) ** (-0.5)
    fields = jnp.stack(
        [lax.all_gather(volume, "col", axis=0, tiled=True),
         lax.all_gather(upstream, "col", axis=0, tiled=True)]
    )
    all_rows = lax.all_gather(filters, "col", axis=0, tiled=True)
    both = with_halo_2d(fields, 3, 4)
    both = jnp.pad(both, ((0, 0), (0, 0), (1, 1), (0, 0), (0, 0)))
    padded, padded_up = both[0], both[1]
    taps = patches(padded, planes, rows_x, rows_y, False)
    local_grad = jnp.einsum("opqy,kcpqy->ock", upstream, taps, precision=lax.Precision.HIGH)
    local_grad = local_grad.reshape(local_grad.shape[0], local_grad.shape[1], 3, 3, 3)
    flat = local_grad.reshape(-1, 128)
    sizes = [lax.axis_size(a) for a in ("gx", "gy")]
    if all(n & (n - 1) == 0 for n in sizes):
        flat = butterfly_sum(flat, ("gx", "gy"))
    else:
        flat = lax.psum(flat, ("gx", "gy"))
    total_grad = flat.reshape(local_grad.shape)
    by_tap = jnp.swapaxes(filters.reshape(filters.shape[0], filters.shape[1], 27), 1, 2)
    response = jnp.einsum("okc,kcpqy->opqy", by_tap, taps, precision=lax.Precision.HIGH)
    first = lax.axis_index("col") * own_inputs
    own_filters = lax.dynamic_slice_in_dim(all_rows, first, own_inputs, 1)
    own_by_tap = jnp.swapaxes(own_filters.reshape(own_filters.shape[0], own_inputs, 27), 1, 2)
    taps_up = patches(padded_up, planes, rows_x, rows_y, True)
    input_grad = jnp.einsum("okc,kopqy->cpqy", own_by_tap, taps_up, precision=lax.Precision.HIGH)
    return (response, input_grad, total_grad * scale)


def solution(mesh):
    placed = (
        P("col", None, "gx", "gy"),
        P("col", None, None, None, None),
        P("col", None, "gx", "gy"),
    )
    return jax.shard_map(
        shards,
        mesh=mesh,
        in_specs=placed,
        out_specs=(
            P("col", None, "gx", "gy"),
            P("col", None, "gx", "gy"),
            P("col", None, None, None, None),
        ),
        check_vma=False,
    )
```

```python
import jax
import jax.numpy as jnp
from jax import lax
from jax.sharding import PartitionSpec as P


def with_halo(block, sides, width):
    for axis, dim in sides:
        count = lax.axis_size(axis)
        forward = [(i, i + 1) for i in range(count - 1)]
        backward = [(target, source) for source, target in forward]
        low = lax.ppermute(
            lax.slice_in_dim(block, block.shape[dim] - width, None, axis=dim), axis, forward
        )
        high = lax.ppermute(lax.slice_in_dim(block, 0, width, axis=dim), axis, backward)
        block = jnp.concatenate([low, block, high], axis=dim)
    return block


def butterfly_sum(value, axes):
    for axis in axes:
        count = lax.axis_size(axis)
        index = lax.axis_index(axis)
        stride = 1
        while stride < count:
            radix = 4 if (count // stride) % 4 == 0 else 2
            member = (index // stride) % radix
            received = [value]
            for shift in range(1, radix):
                pairs = []
                for i in range(count):
                    m = (i // stride) % radix
                    j = i + (((m + shift) % radix) - m) * stride
                    pairs.append((i, j))
                received.append(lax.ppermute(value, axis, pairs))
            stacked = jnp.stack(received)
            ordered = jnp.take(stacked, (member - jnp.arange(radix)) % radix, axis=0)
            parts = [ordered[m] for m in range(radix)]
            while len(parts) > 1:
                parts = [parts[k] + parts[k + 1] for k in range(0, len(parts), 2)]
            value = parts[0]
            stride *= radix
    return value


def pad_depth(field):
    return jnp.pad(field, ((0, 0), (1, 1), (0, 0), (0, 0)))


def patches(field, planes, rows_x, rows_y, flip):
    windows = []
    for depth in range(3):
        for across in range(3):
            for along in range(3):
                a, b, e = (2 - depth, 2 - across, 2 - along) if flip else (depth, across, along)
                windows.append(field[:, a : a + planes, b : b + rows_x, e : e + rows_y])
    return jnp.stack(windows, axis=0)


def shards(volume, filters, upstream):
    channels, planes, rows_x, rows_y = volume.shape
    own_inputs = channels
    ncol = lax.axis_size("col")
    scale = (planes * rows_x * lax.axis_size("gx") * rows_y * lax.axis_size("gy")) ** (-0.5)
    fields = jnp.stack(
        [lax.all_gather(volume, "col", axis=0, tiled=True),
         lax.all_gather(upstream, "col", axis=0, tiled=True)]
    )
    all_rows = lax.all_gather(filters, "col", axis=0, tiled=True)
    both = with_halo(fields, (("gx", 3), ("gy", 4)), 1)
    both = jnp.pad(both, ((0, 0), (0, 0), (1, 1), (0, 0), (0, 0)))
    padded, padded_up = both[0], both[1]
    taps = patches(padded, planes, rows_x, rows_y, False)
    first = lax.axis_index("col") * own_inputs
    own_up = lax.dynamic_slice_in_dim(padded_up, first, own_inputs, 0)
    shifted_up = patches(own_up, planes, rows_x, rows_y, True)
    local_grad = jnp.einsum("kopqy,cpqy->ock", shifted_up, fields[0], precision=lax.Precision.HIGH)
    local_grad = local_grad.reshape(local_grad.shape[0], local_grad.shape[1], 3, 3, 3)
    flat = local_grad.reshape(-1, 128)
    sizes = [lax.axis_size(a) for a in ("gx", "gy")]
    if all(n & (n - 1) == 0 for n in sizes):
        flat = butterfly_sum(flat, ("gx", "gy"))
    else:
        flat = lax.psum(flat, ("gx", "gy"))
    total_grad = flat.reshape(local_grad.shape)
    by_tap = jnp.swapaxes(filters.reshape(filters.shape[0], filters.shape[1], 27), 1, 2)
    response = jnp.einsum("okc,kcpqy->opqy", by_tap, taps, precision=lax.Precision.HIGH)
    own_filters = lax.dynamic_slice_in_dim(all_rows, first, own_inputs, 1)
    own_by_tap = jnp.swapaxes(own_filters.reshape(own_filters.shape[0], own_inputs, 27), 1, 2)
    taps_up = patches(padded_up, planes, rows_x, rows_y, True)
    input_grad = jnp.einsum("okc,kopqy->cpqy", own_by_tap, taps_up, precision=lax.Precision.HIGH)
    return (response, input_grad, total_grad * scale)


def solution(mesh):
    placed = (
        P("col", None, "gx", "gy"),
        P("col", None, None, None, None),
        P("col", None, "gx", "gy"),
    )
    return jax.shard_map(
        shards,
        mesh=mesh,
        in_specs=placed,
        out_specs=(
            P("col", None, "gx", "gy"),
            P("col", None, "gx", "gy"),
            P("col", None, None, None, None),
        ),
        check_vma=False,
    )
```

```python
import jax
import jax.numpy as jnp
from jax import lax
from jax.sharding import PartitionSpec as P


def with_halo(block, sides, width):
    for axis, dim in sides:
        count = lax.axis_size(axis)
        forward = [(i, i + 1) for i in range(count - 1)]
        backward = [(target, source) for source, target in forward]
        low = lax.ppermute(
            lax.slice_in_dim(block, block.shape[dim] - width, None, axis=dim), axis, forward
        )
        high = lax.ppermute(lax.slice_in_dim(block, 0, width, axis=dim), axis, backward)
        block = jnp.concatenate([low, block, high], axis=dim)
    return block


def butterfly_sum(value, axes):
    for axis in axes:
        count = lax.axis_size(axis)
        index = lax.axis_index(axis)
        stride = 1
        while stride < count:
            radix = 4 if (count // stride) % 4 == 0 else 2
            member = (index // stride) % radix
            received = [value]
            for shift in range(1, radix):
                pairs = []
                for i in range(count):
                    m = (i // stride) % radix
                    j = i + (((m + shift) % radix) - m) * stride
                    pairs.append((i, j))
                received.append(lax.ppermute(value, axis, pairs))
            stacked = jnp.stack(received)
            ordered = jnp.take(stacked, (member - jnp.arange(radix)) % radix, axis=0)
            parts = [ordered[m] for m in range(radix)]
            while len(parts) > 1:
                parts = [parts[k] + parts[k + 1] for k in range(0, len(parts), 2)]
            value = parts[0]
            stride *= radix
    return value


def pad_depth(field):
    return jnp.pad(field, ((0, 0), (1, 1), (0, 0), (0, 0)))


def patches(field, planes, rows_x, rows_y, flip):
    windows = []
    for depth in range(3):
        for across in range(3):
            for along in range(3):
                a, b, e = (2 - depth, 2 - across, 2 - along) if flip else (depth, across, along)
                windows.append(field[:, a : a + planes, b : b + rows_x, e : e + rows_y])
    return jnp.stack(windows, axis=0)


def shards(volume, filters, upstream):
    channels, planes, rows_x, rows_y = volume.shape
    own_inputs = channels
    ncol = lax.axis_size("col")
    scale = (planes * rows_x * lax.axis_size("gx") * rows_y * lax.axis_size("gy")) ** (-0.5)
    gathered = lax.all_gather(volume, "col", axis=0, tiled=True)
    fields = jnp.stack([gathered, lax.all_gather(upstream, "col", axis=0, tiled=True)])
    all_rows = lax.all_gather(filters, "col", axis=0, tiled=True)
    both = with_halo(fields, (("gx", 3), ("gy", 4)), 1)
    both = jnp.pad(both, ((0, 0), (0, 0), (1, 1), (0, 0), (0, 0)))
    padded, padded_up = both[0], both[1]
    taps = patches(padded, planes, rows_x, rows_y, False)
    own_up = pad_depth(with_halo(upstream, (("gx", 2), ("gy", 3)), 1))
    shifted_up = patches(own_up, planes, rows_x, rows_y, True)
    local_grad = jnp.einsum("kopqy,cpqy->ock", shifted_up, gathered, precision=lax.Precision.HIGH)
    local_grad = local_grad.reshape(local_grad.shape[0], local_grad.shape[1], 3, 3, 3)
    flat = local_grad.reshape(-1, 128)
    sizes = [lax.axis_size(a) for a in ("gx", "gy")]
    if all(n & (n - 1) == 0 for n in sizes):
        flat = butterfly_sum(flat, ("gx", "gy"))
    else:
        flat = lax.psum(flat, ("gx", "gy"))
    total_grad = flat.reshape(local_grad.shape)
    by_tap = jnp.swapaxes(filters.reshape(filters.shape[0], filters.shape[1], 27), 1, 2)
    response = jnp.einsum("okc,kcpqy->opqy", by_tap, taps, precision=lax.Precision.HIGH)
    first = lax.axis_index("col") * own_inputs
    own_filters = lax.dynamic_slice_in_dim(all_rows, first, own_inputs, 1)
    own_by_tap = jnp.swapaxes(own_filters.reshape(own_filters.shape[0], own_inputs, 27), 1, 2)
    taps_up = patches(padded_up, planes, rows_x, rows_y, True)
    input_grad = jnp.einsum("okc,kopqy->cpqy", own_by_tap, taps_up, precision=lax.Precision.HIGH)
    return (response, input_grad, total_grad * scale)


def solution(mesh):
    placed = (
        P("col", None, "gx", "gy"),
        P("col", None, None, None, None),
        P("col", None, "gx", "gy"),
    )
    return jax.shard_map(
        shards,
        mesh=mesh,
        in_specs=placed,
        out_specs=(
            P("col", None, "gx", "gy"),
            P("col", None, "gx", "gy"),
            P("col", None, None, None, None),
        ),
        check_vma=False,
    )
```

```python
import jax
import jax.numpy as jnp
from jax import lax
from jax.sharding import PartitionSpec as P


def with_halo(block, sides, width):
    for axis, dim in sides:
        count = lax.axis_size(axis)
        forward = [(i, i + 1) for i in range(count - 1)]
        backward = [(target, source) for source, target in forward]
        low = lax.ppermute(
            lax.slice_in_dim(block, block.shape[dim] - width, None, axis=dim), axis, forward
        )
        high = lax.ppermute(lax.slice_in_dim(block, 0, width, axis=dim), axis, backward)
        block = jnp.concatenate([low, block, high], axis=dim)
    return block


def butterfly_sum(value, axes):
    for axis in axes:
        count = lax.axis_size(axis)
        index = lax.axis_index(axis)
        stride = 1
        while stride < count:
            radix = 4 if (count // stride) % 4 == 0 else 2
            member = (index // stride) % radix
            received = [value]
            for shift in range(1, radix):
                pairs = []
                for i in range(count):
                    m = (i // stride) % radix
                    j = i + (((m + shift) % radix) - m) * stride
                    pairs.append((i, j))
                received.append(lax.ppermute(value, axis, pairs))
            stacked = jnp.stack(received)
            ordered = jnp.take(stacked, (member - jnp.arange(radix)) % radix, axis=0)
            parts = [ordered[m] for m in range(radix)]
            while len(parts) > 1:
                parts = [parts[k] + parts[k + 1] for k in range(0, len(parts), 2)]
            value = parts[0]
            stride *= radix
    return value


def pad_depth(field):
    return jnp.pad(field, ((0, 0), (1, 1), (0, 0), (0, 0)))


def patches(field, planes, rows_x, rows_y, flip):
    windows = []
    for depth in range(3):
        for across in range(3):
            for along in range(3):
                a, b, e = (2 - depth, 2 - across, 2 - along) if flip else (depth, across, along)
                windows.append(field[:, a : a + planes, b : b + rows_x, e : e + rows_y])
    return jnp.stack(windows, axis=0)


def scatter_sum(blocks, axis):
    count = lax.axis_size(axis)
    index = lax.axis_index(axis)
    blocks = blocks.reshape((count, blocks.shape[0] // count) + blocks.shape[1:])
    total = blocks[index]
    for shift in range(1, count):
        piece = blocks[(index + shift) % count]
        pairs = [(i, (i + shift) % count) for i in range(count)]
        total = total + lax.ppermute(piece, axis, pairs)
    return total


def shards(volume, filters, upstream):
    channels, planes, rows_x, rows_y = volume.shape
    scale = (planes * rows_x * lax.axis_size("gx") * rows_y * lax.axis_size("gy")) ** (-0.5)
    gathered = lax.all_gather(volume, "col", axis=0, tiled=True)
    padded = pad_depth(with_halo(gathered, (("gx", 2), ("gy", 3)), 1))
    own_up = pad_depth(with_halo(upstream, (("gx", 2), ("gy", 3)), 1))
    shifted_up = patches(own_up, planes, rows_x, rows_y, True)
    local_grad = jnp.einsum("kopqy,cpqy->ock", shifted_up, gathered, precision=lax.Precision.HIGH)
    local_grad = local_grad.reshape(local_grad.shape[0], local_grad.shape[1], 3, 3, 3)
    flat = local_grad.reshape(-1, 128)
    sizes = [lax.axis_size(a) for a in ("gx", "gy")]
    if all(n & (n - 1) == 0 for n in sizes):
        flat = butterfly_sum(flat, ("gx", "gy"))
    else:
        flat = lax.psum(flat, ("gx", "gy"))
    total_grad = flat.reshape(local_grad.shape)
    taps = patches(padded, planes, rows_x, rows_y, False)
    by_tap = jnp.swapaxes(filters.reshape(filters.shape[0], filters.shape[1], 27), 1, 2)
    response = jnp.einsum("okc,kcpqy->opqy", by_tap, taps, precision=lax.Precision.HIGH)
    partial = jnp.einsum("okc,kopqy->cpqy", by_tap, shifted_up, precision=lax.Precision.HIGH)
    input_grad = scatter_sum(partial, "col")
    return (response, input_grad, total_grad * scale)


def solution(mesh):
    placed = (
        P("col", None, "gx", "gy"),
        P("col", None, None, None, None),
        P("col", None, "gx", "gy"),
    )
    return jax.shard_map(
        shards,
        mesh=mesh,
        in_specs=placed,
        out_specs=(
            P("col", None, "gx", "gy"),
            P("col", None, "gx", "gy"),
            P("col", None, None, None, None),
        ),
        check_vma=False,
    )
```

```python
import jax
import jax.numpy as jnp
from jax import lax
from jax.sharding import PartitionSpec as P


def with_halo(block, sides, width):
    for axis, dim in sides:
        count = lax.axis_size(axis)
        forward = [(i, i + 1) for i in range(count - 1)]
        backward = [(target, source) for source, target in forward]
        low = lax.ppermute(
            lax.slice_in_dim(block, block.shape[dim] - width, None, axis=dim), axis, forward
        )
        high = lax.ppermute(lax.slice_in_dim(block, 0, width, axis=dim), axis, backward)
        block = jnp.concatenate([low, block, high], axis=dim)
    return block


def butterfly_sum(value, axes):
    for axis in axes:
        count = lax.axis_size(axis)
        index = lax.axis_index(axis)
        stride = 1
        while stride < count:
            left = count // stride
            radix = 8 if left == 8 else (4 if left % 4 == 0 else 2)
            member = (index // stride) % radix
            received = [value]
            for shift in range(1, radix):
                pairs = []
                for i in range(count):
                    m = (i // stride) % radix
                    j = i + (((m + shift) % radix) - m) * stride
                    pairs.append((i, j))
                received.append(lax.ppermute(value, axis, pairs))
            stacked = jnp.stack(received)
            ordered = jnp.take(stacked, (member - jnp.arange(radix)) % radix, axis=0)
            parts = [ordered[m] for m in range(radix)]
            while len(parts) > 1:
                parts = [parts[k] + parts[k + 1] for k in range(0, len(parts), 2)]
            value = parts[0]
            stride *= radix
    return value


def pad_depth(field):
    return jnp.pad(field, ((0, 0), (1, 1), (0, 0), (0, 0)))


def patches(field, planes, rows_x, rows_y, flip):
    windows = []
    for depth in range(3):
        for across in range(3):
            for along in range(3):
                a, b, e = (2 - depth, 2 - across, 2 - along) if flip else (depth, across, along)
                windows.append(field[:, a : a + planes, b : b + rows_x, e : e + rows_y])
    return jnp.stack(windows, axis=0)


def shards(volume, filters, upstream):
    channels, planes, rows_x, rows_y = volume.shape
    own_inputs = channels
    ncol = lax.axis_size("col")
    scale = (planes * rows_x * lax.axis_size("gx") * rows_y * lax.axis_size("gy")) ** (-0.5)
    fields = jnp.stack(
        [lax.all_gather(volume, "col", axis=0, tiled=True),
         lax.all_gather(upstream, "col", axis=0, tiled=True)]
    )
    all_rows = lax.all_gather(filters, "col", axis=0, tiled=True)
    both = with_halo(fields, (("gx", 3), ("gy", 4)), 1)
    both = jnp.pad(both, ((0, 0), (0, 0), (1, 1), (0, 0), (0, 0)))
    padded, padded_up = both[0], both[1]
    taps = patches(padded, planes, rows_x, rows_y, False)
    first = lax.axis_index("col") * own_inputs
    own_up = lax.dynamic_slice_in_dim(padded_up, first, own_inputs, 0)
    shifted_up = patches(own_up, planes, rows_x, rows_y, True)
    local_grad = jnp.einsum("kopqy,cpqy->ock", shifted_up, fields[0], precision=lax.Precision.HIGH)
    local_grad = local_grad.reshape(local_grad.shape[0], local_grad.shape[1], 3, 3, 3)
    flat = local_grad.reshape(-1, 128)
    sizes = [lax.axis_size(a) for a in ("gx", "gy")]
    if all(n & (n - 1) == 0 for n in sizes):
        flat = butterfly_sum(flat, ("gx", "gy"))
    else:
        flat = lax.psum(flat, ("gx", "gy"))
    total_grad = flat.reshape(local_grad.shape)
    by_tap = jnp.swapaxes(filters.reshape(filters.shape[0], filters.shape[1], 27), 1, 2)
    response = jnp.einsum("okc,kcpqy->opqy", by_tap, taps, precision=lax.Precision.HIGH)
    own_filters = lax.dynamic_slice_in_dim(all_rows, first, own_inputs, 1)
    own_by_tap = jnp.swapaxes(own_filters.reshape(own_filters.shape[0], own_inputs, 27), 1, 2)
    taps_up = patches(padded_up, planes, rows_x, rows_y, True)
    input_grad = jnp.einsum("okc,kopqy->cpqy", own_by_tap, taps_up, precision=lax.Precision.HIGH)
    return (response, input_grad, total_grad * scale)


def solution(mesh):
    placed = (
        P("col", None, "gx", "gy"),
        P("col", None, None, None, None),
        P("col", None, "gx", "gy"),
    )
    return jax.shard_map(
        shards,
        mesh=mesh,
        in_specs=placed,
        out_specs=(
            P("col", None, "gx", "gy"),
            P("col", None, "gx", "gy"),
            P("col", None, None, None, None),
        ),
        check_vma=False,
    )
```

```python
import jax
import jax.numpy as jnp
from jax import lax
from jax.sharding import PartitionSpec as P


def with_halo(block, sides, width):
    for axis, dim in sides:
        count = lax.axis_size(axis)
        forward = [(i, i + 1) for i in range(count - 1)]
        backward = [(target, source) for source, target in forward]
        low = lax.ppermute(
            lax.slice_in_dim(block, block.shape[dim] - width, None, axis=dim), axis, forward
        )
        high = lax.ppermute(lax.slice_in_dim(block, 0, width, axis=dim), axis, backward)
        block = jnp.concatenate([low, block, high], axis=dim)
    return block


def butterfly_sum(value, axes):
    for axis in axes:
        count = lax.axis_size(axis)
        index = lax.axis_index(axis)
        stride = 1
        while stride < count:
            radix = 4 if (count // stride) % 4 == 0 else 2
            member = (index // stride) % radix
            received = [value]
            for shift in range(1, radix):
                pairs = []
                for i in range(count):
                    m = (i // stride) % radix
                    j = i + (((m + shift) % radix) - m) * stride
                    pairs.append((i, j))
                received.append(lax.ppermute(value, axis, pairs))
            stacked = jnp.stack(received)
            ordered = jnp.take(stacked, (member - jnp.arange(radix)) % radix, axis=0)
            parts = [ordered[m] for m in range(radix)]
            while len(parts) > 1:
                parts = [parts[k] + parts[k + 1] for k in range(0, len(parts), 2)]
            value = parts[0]
            stride *= radix
    return value


def pad_depth(field):
    return jnp.pad(field, ((0, 0), (1, 1), (0, 0), (0, 0)))


def patches(field, planes, rows_x, rows_y, flip):
    windows = []
    for depth in range(3):
        for across in range(3):
            for along in range(3):
                a, b, e = (2 - depth, 2 - across, 2 - along) if flip else (depth, across, along)
                windows.append(field[:, a : a + planes, b : b + rows_x, e : e + rows_y])
    return jnp.stack(windows, axis=0)


def shards(volume, filters, upstream):
    channels, planes, rows_x, rows_y = volume.shape
    own_inputs = channels
    ncol = lax.axis_size("col")
    scale = (planes * rows_x * lax.axis_size("gx") * rows_y * lax.axis_size("gy")) ** (-0.5)
    fields = jnp.stack(
        [lax.all_gather(volume, "col", axis=0, tiled=True),
         lax.all_gather(upstream, "col", axis=0, tiled=True)]
    )
    all_rows = lax.all_gather(filters, "col", axis=0, tiled=True)
    both = with_halo(fields, (("gx", 3), ("gy", 4)), 1)
    both = jnp.pad(both, ((0, 0), (0, 0), (1, 1), (0, 0), (0, 0)))
    padded, padded_up = both[0], both[1]
    taps = patches(padded, planes, rows_x, rows_y, False)
    first = lax.axis_index("col") * own_inputs
    own_up = lax.dynamic_slice_in_dim(padded_up, first, own_inputs, 0)
    shifted_up = patches(own_up, planes, rows_x, rows_y, True)
    local_grad = jnp.einsum("kopqy,cpqy->ock", shifted_up, fields[0], precision=lax.Precision.HIGH)
    local_grad = local_grad.reshape(local_grad.shape[0], local_grad.shape[1], 3, 3, 3)
    flat = local_grad.reshape(-1, 128)
    sizes = [lax.axis_size(a) for a in ("gx", "gy")]
    if all(n & (n - 1) == 0 for n in sizes):
        flat = butterfly_sum(flat, ("gy", "gx"))
    else:
        flat = lax.psum(flat, ("gx", "gy"))
    total_grad = flat.reshape(local_grad.shape)
    by_tap = jnp.swapaxes(filters.reshape(filters.shape[0], filters.shape[1], 27), 1, 2)
    response = jnp.einsum("okc,kcpqy->opqy", by_tap, taps, precision=lax.Precision.HIGH)
    own_filters = lax.dynamic_slice_in_dim(all_rows, first, own_inputs, 1)
    own_by_tap = jnp.swapaxes(own_filters.reshape(own_filters.shape[0], own_inputs, 27), 1, 2)
    taps_up = patches(padded_up, planes, rows_x, rows_y, True)
    input_grad = jnp.einsum("okc,kopqy->cpqy", own_by_tap, taps_up, precision=lax.Precision.HIGH)
    return (response, input_grad, total_grad * scale)


def solution(mesh):
    placed = (
        P("col", None, "gx", "gy"),
        P("col", None, None, None, None),
        P("col", None, "gx", "gy"),
    )
    return jax.shard_map(
        shards,
        mesh=mesh,
        in_specs=placed,
        out_specs=(
            P("col", None, "gx", "gy"),
            P("col", None, "gx", "gy"),
            P("col", None, None, None, None),
        ),
        check_vma=False,
    )
```
